1024 devices in a mesh: bra: 16 (over z), ket: 64 (over y, x, core).
Axes of the slice: x: 4, y: 8, z: 16, core: 2. Of those that a mesh axis runs over, the one named last changes fastest.
Arguments:
- integrals: float32 [3072, 512, 512], P(('bra', 'ket')), may hold values from -0.046875 to 0.046875
- tile_place: int32 [3072, 2], P(('bra', 'ket')), may hold values from -1 to 63, as said below
- amplitudes: float32 [256, 32768], P('bra', 'ket'), may hold values from -6 to 6
- denominators: float32 [256, 32768], P('ket', 'bra'), may hold values from 1 to 4
Outputs:
- new_amplitudes: float32 [256, 32768], P('ket', 'bra')
The draws below stay inside these ranges and needn't reach their ends.
Inputs may be any that keep to these rules, and one draw needn't show every extreme that they name: `tile_place`: device d = b * 64 + k (b its bra index, k its ket index) holds slots d * 3 to (d + 1) * 3 - 1. They list the nonzero tiles of its region, block rows b * 4 to (b + 1) * 4 - 1 and block columns k * 1 to (k + 1) - 1, in row-major order, followed by slots holding -1 in both entries. Every tile appears at most once. In every draw some device has all 3 slots filled.
All inputs are finite; a program needn't handle non-finite values.
Results may differ from the reference program's by a relative error of at most 0.0003.
Values sent between devices are 32-bit elements; how exact they have to be, the bound alone decides.
No kernel may reach another device: no remote copies, remote signals or barrier semaphores. Data moves between devices by JAX's collectives and lax.ppermute only.
A program may use at most 32 MiB of HBM per device.

```python
import jax
import jax.numpy as jnp
from jax import lax

TILE = 512
NBLK = 64
OCC = 256
RB = 4
CB = 1
SLOTS = 3
NPAIR = 32768
N_BRA = 16
N_KET = 64


def tile_live(key):
    region = RB * CB
    device_count = N_BRA * N_KET
    live_bits = jax.random.randint(jax.random.fold_in(key, 11), (device_count, region), 0, 2)
    chosen = jax.random.randint(jax.random.fold_in(key, 12), (), 0, device_count)
    device_ids = jnp.arange(device_count)
    live_bits = jnp.where((device_ids == chosen)[:, None], 1, live_bits)
    live_ranks = jnp.cumsum(live_bits, axis=1)
    return live_bits * (live_ranks <= SLOTS).astype(jnp.int32)


def draw_tile_place(key, part):
    live_bits = tile_live(key)
    device_count = N_BRA * N_KET
    slot_order = jnp.argsort(1 - live_bits, axis=1, stable=True)
    sorted_live = jnp.take_along_axis(live_bits, slot_order, axis=1)[:, :SLOTS]
    sorted_pos = slot_order[:, :SLOTS]
    device_ids = jnp.arange(device_count)
    bra_ids = device_ids // N_KET
    ket_ids = device_ids % N_KET
    block_rows = bra_ids[:, None] * RB + sorted_pos // CB
    block_cols = ket_ids[:, None] * CB + sorted_pos % CB
    block_rows = jnp.where(sorted_live == 1, block_rows, -1)
    block_cols = jnp.where(sorted_live == 1, block_cols, -1)
    return jnp.stack([block_rows, block_cols], axis=-1).reshape(device_count * SLOTS, 2).astype(jnp.int32)


def block_levels(key, dims, cuts, least, largest):
    def one(axis_at, shards_of):
        draws = jax.random.uniform(jax.random.fold_in(jax.random.fold_in(key, 6), axis_at), (shards_of,), jnp.float32, least / len(cuts), largest / len(cuts))
        return jnp.repeat(jnp.exp(draws), dims[axis_at] // shards_of).reshape((-1,) + (1,) * (len(dims) - axis_at - 1))

    factor_of = one(*cuts[0])
    for cut in cuts[1:]:
        factor_of = factor_of * one(*cut)
    return factor_of


def scatter_about(stream_key, shape, deviation, bound, shards=(), dtype=jnp.bfloat16):
    result = jax.random.normal(stream_key, shape, jnp.float32) * deviation
    if len(shards) > 0:
        result = block_levels(stream_key, shape, shards, -0.22, 0.18) * result
    return jnp.clip(result, min=-bound, max=bound).astype(dtype)


def setup_inputs(seed: int = 0) -> dict:
    arg_keys = jax.random.split(jax.random.key(seed), 5)
    return {
        "integrals": scatter_about(arg_keys[0], (N_BRA * N_KET * SLOTS, TILE, TILE), (TILE * NBLK // 2) ** -0.5, 0.046875, ((0, 1024),), jnp.float32),
        "tile_place": draw_tile_place(jax.random.fold_in(arg_keys[4], 71), 0),
        "amplitudes": scatter_about(arg_keys[2], (OCC, NPAIR), 1.0, 6.0, ((0, 16), (1, 64)), jnp.float32),
        "denominators": jnp.clip(1.0 + 3.0 * jax.random.uniform(arg_keys[3], (OCC, NPAIR), jnp.float32) ** block_levels(arg_keys[3], (OCC, NPAIR), ((0, 64), (1, 16)), -0.2, 0.2), 1.0, 4.0),
    }


def reference(integrals, tile_place, amplitudes, denominators):
    empty_ladder = jnp.zeros((OCC, NBLK * TILE), jnp.float32)

    def visit_slot(ladder, slot_data):
        tile_now, placement = slot_data
        block_row = placement[0].astype(jnp.int32)
        block_col = jnp.maximum(placement[1], 0).astype(jnp.int32)

        def add_tile(ladder_now):
            amp_block = lax.dynamic_slice_in_dim(amplitudes, (block_col * TILE).astype(jnp.int32), TILE, 1)
            tile_product = lax.dot_general(amp_block, tile_now, (((1,), (1,)), ((), ())), precision=lax.Precision.HIGHEST, preferred_element_type=jnp.float32)
            offset = (jnp.maximum(block_row, 0) * TILE).astype(jnp.int32)
            current = lax.dynamic_slice_in_dim(ladder_now, offset, TILE, 1)
            return lax.dynamic_update_slice_in_dim(ladder_now, current + tile_product, offset, 1)

        def keep_same(ladder_now):
            return ladder_now

        return lax.cond(block_row >= 0, add_tile, keep_same, ladder), None

    ladder, unused = lax.scan(visit_slot, empty_ladder, (integrals, tile_place))
    return ladder / denominators
```

```python
import jax
import jax.numpy as jnp
from jax import lax
from jax.sharding import PartitionSpec as P

RS_MINOR = 256


def tile_term(amp_block, tile_now):
    return lax.dot_general(
        amp_block,
        tile_now,
        (((1,), (1,)), ((), ())),
        precision=lax.Precision.HIGHEST,
        preferred_element_type=jnp.float32,
    )


def partial_rows(gathered, integrals, local_rows, row_blocks):
    products = [tile_term(gathered, integrals[s]) for s in range(integrals.shape[0])]
    blocks = []
    for r in range(row_blocks):
        acc = jnp.zeros_like(products[0])
        for s, product in enumerate(products):
            acc = acc + jnp.where(local_rows[s] == r, product, 0.0)
        blocks.append(acc)
    return jnp.concatenate(blocks, axis=1)


def per_device(integrals, tile_place, amplitudes, denominators):
    tile_width = integrals.shape[1]
    row_blocks = denominators.shape[1] // tile_width
    local_rows = tile_place[:, 0] - lax.axis_index("bra") * row_blocks
    gathered = lax.all_gather(amplitudes, "bra", axis=0, tiled=True)
    partial = partial_rows(gathered, integrals, local_rows, row_blocks)
    occ, width = partial.shape
    summed = lax.psum_scatter(
        partial.reshape(occ * width // RS_MINOR, RS_MINOR), "ket", scatter_dimension=0, tiled=True
    )
    return summed.reshape(denominators.shape) / denominators


def solution(mesh):
    placed = (
        P(("bra", "ket"), None, None),
        P(("bra", "ket"), None),
        P("bra", "ket"),
        P("ket", "bra"),
    )
    return jax.shard_map(
        per_device, mesh=mesh, in_specs=placed, out_specs=P("ket", "bra"), check_vma=False
    )
```

```python
import jax
import jax.numpy as jnp
from jax import lax
from jax.sharding import PartitionSpec as P

RS_MINOR = 256


def tile_term(amp_block, tile_now):
    return lax.dot_general(
        amp_block,
        tile_now,
        (((1,), (1,)), ((), ())),
        precision=lax.Precision.HIGHEST,
        preferred_element_type=jnp.float32,
    )


def partial_rows(gathered, integrals, local_rows, row_blocks):
    products = [tile_term(gathered, integrals[s]) for s in range(integrals.shape[0])]
    blocks = []
    for r in range(row_blocks):
        acc = jnp.zeros_like(products[0])
        for s, product in enumerate(products):
            acc = acc + jnp.where(local_rows[s] == r, product, 0.0)
        blocks.append(acc)
    return jnp.concatenate(blocks, axis=1)


CHIP_X = 4
CORES = 2


def shifted(value, offset, size, stride, n):
    pairs = []
    for k in range(n):
        coord = (k // stride) % size
        dest = k + (((coord + offset) % size) - coord) * stride
        pairs.append((k, dest))
    return lax.ppermute(value, "ket", perm=pairs)


def reduce_ket(partial):
    n = lax.axis_size("ket")
    n_y = n // (CHIP_X * CORES)
    k = lax.axis_index("ket")
    c = k % CORES
    x = (k // CORES) % CHIP_X
    y = k // (CORES * CHIP_X)
    parts = partial.reshape(n_y, CHIP_X, CORES, -1, RS_MINOR)
    keep = lax.dynamic_index_in_dim(parts, c, axis=2, keepdims=False)
    send = lax.dynamic_index_in_dim(parts, 1 - c, axis=2, keepdims=False)
    stage = keep + shifted(send, 1, CORES, 1, n)
    total = lax.dynamic_index_in_dim(stage, x, axis=1, keepdims=False)
    for s in range(1, CHIP_X):
        piece = lax.dynamic_index_in_dim(stage, (x + s) % CHIP_X, axis=1, keepdims=False)
        total = total + shifted(piece, s, CHIP_X, CORES, n)
    stage = total
    total = lax.dynamic_index_in_dim(stage, y, axis=0, keepdims=False)
    for s in range(1, n_y):
        piece = lax.dynamic_index_in_dim(stage, (y + s) % n_y, axis=0, keepdims=False)
        total = total + shifted(piece, s, n_y, CORES * CHIP_X, n)
    return total

def per_device(integrals, tile_place, amplitudes, denominators):
    tile_width = integrals.shape[1]
    row_blocks = denominators.shape[1] // tile_width
    local_rows = tile_place[:, 0] - lax.axis_index("bra") * row_blocks
    gathered = lax.all_gather(amplitudes, "bra", axis=0, tiled=True)
    partial = partial_rows(gathered, integrals, local_rows, row_blocks)
    occ, width = partial.shape
    summed = reduce_ket(partial)
    return summed.reshape(denominators.shape) / denominators


def solution(mesh):
    placed = (
        P(("bra", "ket"), None, None),
        P(("bra", "ket"), None),
        P("bra", "ket"),
        P("ket", "bra"),
    )
    return jax.shard_map(
        per_device, mesh=mesh, in_specs=placed, out_specs=P("ket", "bra"), check_vma=False
    )
```

```python
import jax
import jax.numpy as jnp
from jax import lax
from jax.sharding import Mesh, PartitionSpec as P

RS_MINOR = 256
CHIP_X = 4
CORES = 2
KET = ("y", "x", "core")


def tile_term(amp_block, tile_now):
    return lax.dot_general(
        amp_block,
        tile_now,
        (((1,), (1,)), ((), ())),
        precision=lax.Precision.HIGHEST,
        preferred_element_type=jnp.float32,
    )


def partial_rows(gathered, integrals, local_rows, row_blocks):
    products = [tile_term(gathered, integrals[s]) for s in range(integrals.shape[0])]
    blocks = []
    for r in range(row_blocks):
        acc = jnp.zeros_like(products[0])
        for s, product in enumerate(products):
            acc = acc + jnp.where(local_rows[s] == r, product, 0.0)
        blocks.append(acc)
    return jnp.concatenate(blocks, axis=1)


def gather_bra(amplitudes):
    return lax.all_gather(amplitudes, "bra", axis=0, tiled=True)


def reduce_ket(partial):
    n_y, n_x, n_c = (lax.axis_size(a) for a in KET)
    c = lax.axis_index("core")
    parts = partial.reshape(n_y, n_x, n_c, -1)
    keep = lax.dynamic_index_in_dim(parts, c, axis=2, keepdims=False)
    send = lax.dynamic_index_in_dim(parts, 1 - c, axis=2, keepdims=False)
    stage = keep + lax.ppermute(send, "core", perm=[(0, 1), (1, 0)])
    got = lax.all_to_all(stage, "x", 1, 1, tiled=True)
    stage = jnp.sum(got, axis=1)
    got = lax.all_to_all(stage, "y", 0, 0, tiled=True)
    return jnp.sum(got, axis=0)


def per_device(integrals, tile_place, amplitudes, denominators):
    tile_width = integrals.shape[1]
    row_blocks = denominators.shape[1] // tile_width
    local_rows = tile_place[:, 0] - lax.axis_index("bra") * row_blocks
    gathered = gather_bra(amplitudes)
    partial = partial_rows(gathered, integrals, local_rows, row_blocks)
    summed = reduce_ket(partial)
    return summed.reshape(denominators.shape) / denominators


def solution(mesh):
    n_bra, n_ket = mesh.devices.shape
    fine = Mesh(mesh.devices.reshape(n_bra, n_ket // (CHIP_X * CORES), CHIP_X, CORES), ("bra",) + KET)
    placed = (
        P(("bra",) + KET, None, None),
        P(("bra",) + KET, None),
        P("bra", KET),
        P(KET, "bra"),
    )
    return jax.shard_map(
        per_device, mesh=fine, in_specs=placed, out_specs=P(KET, "bra"), check_vma=False
    )
```

```python
import jax
import jax.numpy as jnp
from jax import lax
from jax.sharding import Mesh, PartitionSpec as P

RS_MINOR = 256
CHIP_X = 4
CORES = 2
KET = ("y", "x", "core")


def tile_term(amp_block, tile_now):
    return lax.dot_general(
        amp_block,
        tile_now,
        (((1,), (1,)), ((), ())),
        precision=lax.Precision.HIGHEST,
        preferred_element_type=jnp.float32,
    )


def partial_rows(gathered, integrals, local_rows, row_blocks):
    products = [tile_term(gathered, integrals[s]) for s in range(integrals.shape[0])]
    blocks = []
    for r in range(row_blocks):
        acc = jnp.zeros_like(products[0])
        for s, product in enumerate(products):
            acc = acc + jnp.where(local_rows[s] == r, product, 0.0)
        blocks.append(acc)
    return jnp.concatenate(blocks, axis=1)


def gather_bra(amplitudes):
    n_bra = lax.axis_size("bra")
    copies = jnp.broadcast_to(amplitudes[None], (n_bra,) + amplitudes.shape)
    return lax.all_to_all(copies, "bra", 0, 0, tiled=True).reshape(-1, amplitudes.shape[1])


def reduce_ket(partial):
    n_y, n_x, n_c = (lax.axis_size(a) for a in KET)
    c = lax.axis_index("core")
    parts = partial.reshape(n_y, n_x, n_c, -1)
    keep = lax.dynamic_index_in_dim(parts, c, axis=2, keepdims=False)
    send = lax.dynamic_index_in_dim(parts, 1 - c, axis=2, keepdims=False)
    stage = keep + lax.ppermute(send, "core", perm=[(0, 1), (1, 0)])
    got = lax.all_to_all(stage, "x", 1, 1, tiled=True)
    stage = jnp.sum(got, axis=1)
    got = lax.all_to_all(stage, "y", 0, 0, tiled=True)
    return jnp.sum(got, axis=0)


def per_device(integrals, tile_place, amplitudes, denominators):
    tile_width = integrals.shape[1]
    row_blocks = denominators.shape[1] // tile_width
    local_rows = tile_place[:, 0] - lax.axis_index("bra") * row_blocks
    gathered = gather_bra(amplitudes)
    partial = partial_rows(gathered, integrals, local_rows, row_blocks)
    summed = reduce_ket(partial)
    return summed.reshape(denominators.shape) / denominators


def solution(mesh):
    n_bra, n_ket = mesh.devices.shape
    fine = Mesh(mesh.devices.reshape(n_bra, n_ket // (CHIP_X * CORES), CHIP_X, CORES), ("bra",) + KET)
    placed = (
        P(("bra",) + KET, None, None),
        P(("bra",) + KET, None),
        P("bra", KET),
        P(KET, "bra"),
    )
    return jax.shard_map(
        per_device, mesh=fine, in_specs=placed, out_specs=P(KET, "bra"), check_vma=False
    )
```

```python
import jax
import jax.numpy as jnp
from jax import lax
from jax.sharding import Mesh, PartitionSpec as P

RS_MINOR = 256
CHIP_X = 4
CORES = 2
KET = ("y", "x", "core")


def tile_term(amp_block, tile_now):
    return lax.dot_general(
        amp_block,
        tile_now,
        (((1,), (1,)), ((), ())),
        precision=lax.Precision.HIGH,
        preferred_element_type=jnp.float32,
    )


def partial_rows(gathered, integrals, local_rows, row_blocks):
    products = [tile_term(gathered, integrals[s]) for s in range(integrals.shape[0])]
    blocks = []
    for r in range(row_blocks):
        acc = jnp.zeros_like(products[0])
        for s, product in enumerate(products):
            acc = acc + jnp.where(local_rows[s] == r, product, 0.0)
        blocks.append(acc)
    return jnp.concatenate(blocks, axis=1)


def gather_bra(amplitudes):
    n_bra = lax.axis_size("bra")
    copies = jnp.broadcast_to(amplitudes[None], (n_bra,) + amplitudes.shape)
    return lax.all_to_all(copies, "bra", 0, 0, tiled=True).reshape(-1, amplitudes.shape[1])


def reduce_plane(stage):
    got = lax.all_to_all(stage, "x", 1, 1, tiled=True)
    stage = jnp.sum(got, axis=1)
    got = lax.all_to_all(stage, "y", 0, 0, tiled=True)
    return jnp.sum(got, axis=0)


def per_device(integrals, tile_place, amplitudes, denominators):
    tile_width = integrals.shape[1]
    row_blocks = denominators.shape[1] // tile_width
    local_rows = tile_place[:, 0] - lax.axis_index("bra") * row_blocks
    n_y, n_x, n_c = (lax.axis_size(a) for a in KET)
    c = lax.axis_index("core")
    gathered = gather_bra(amplitudes).reshape(n_y, n_x, n_c, -1, tile_width)
    own = lax.dynamic_index_in_dim(gathered, c, axis=2, keepdims=False).reshape(-1, tile_width)
    other = lax.dynamic_index_in_dim(gathered, 1 - c, axis=2, keepdims=False).reshape(-1, tile_width)
    sent = partial_rows(other, integrals, local_rows, row_blocks)
    arrived = lax.ppermute(sent, "core", perm=[(0, 1), (1, 0)])
    stage = partial_rows(own, integrals, local_rows, row_blocks) + arrived
    summed = reduce_plane(stage.reshape(n_y, n_x, -1))
    return summed.reshape(denominators.shape) / denominators


def solution(mesh):
    n_bra, n_ket = mesh.devices.shape
    fine = Mesh(mesh.devices.reshape(n_bra, n_ket // (CHIP_X * CORES), CHIP_X, CORES), ("bra",) + KET)
    placed = (
        P(("bra",) + KET, None, None),
        P(("bra",) + KET, None),
        P("bra", KET),
        P(KET, "bra"),
    )
    return jax.shard_map(
        per_device, mesh=fine, in_specs=placed, out_specs=P(KET, "bra"), check_vma=False
    )
```

```python
import jax
import jax.numpy as jnp
from jax import lax
from jax.sharding import Mesh, PartitionSpec as P

RS_MINOR = 256
CHIP_X = 4
CORES = 2
KET = ("y", "x", "core")


def tile_term(amp_block, tile_now):
    return lax.dot_general(
        amp_block,
        tile_now,
        (((1,), (1,)), ((), ())),
        precision=lax.Precision.HIGH,
        preferred_element_type=jnp.float32,
    )


def partial_rows(gathered, integrals, local_rows, row_blocks):
    products = [tile_term(gathered, integrals[s]) for s in range(integrals.shape[0])]
    blocks = []
    for r in range(row_blocks):
        acc = jnp.zeros_like(products[0])
        for s, product in enumerate(products):
            acc = acc + jnp.where(local_rows[s] == r, product, 0.0)
        blocks.append(acc)
    return jnp.concatenate(blocks, axis=1)


def gather_bra(amplitudes):
    n_bra = lax.axis_size("bra")
    rows, width = amplitudes.shape
    by_core = amplitudes.reshape(2, CORES, rows // (2 * CORES), width)
    by_core = jnp.transpose(by_core, (1, 0, 2, 3)).reshape(CORES, 1, rows // CORES, width)
    copies = jnp.broadcast_to(by_core, (CORES, n_bra, rows // CORES, width))
    return lax.all_to_all(copies, "bra", 1, 1, tiled=True)


def reduce_plane(stage):
    got = lax.all_to_all(jnp.transpose(stage, (1, 0, 2)), "x", 0, 0, tiled=True)
    stage = jnp.sum(got, axis=0)
    got = lax.all_to_all(stage, "y", 0, 0, tiled=True)
    return jnp.sum(got, axis=0)


def per_device(integrals, tile_place, amplitudes, denominators):
    tile_width = integrals.shape[1]
    row_blocks = denominators.shape[1] // tile_width
    local_rows = tile_place[:, 0] - lax.axis_index("bra") * row_blocks
    n_y, n_x, n_c = (lax.axis_size(a) for a in KET)
    c = lax.axis_index("core")
    gathered = gather_bra(amplitudes)
    own = lax.dynamic_index_in_dim(gathered, c, axis=0, keepdims=False).reshape(-1, tile_width)
    other = lax.dynamic_index_in_dim(gathered, 1 - c, axis=0, keepdims=False).reshape(-1, tile_width)
    sent = partial_rows(other, integrals, local_rows, row_blocks)
    arrived = lax.ppermute(sent, "core", perm=[(0, 1), (1, 0)])
    stage = partial_rows(own, integrals, local_rows, row_blocks) + arrived
    summed = reduce_plane(stage.reshape(n_y, n_x, -1))
    return summed.reshape(denominators.shape) / denominators


def solution(mesh):
    n_bra, n_ket = mesh.devices.shape
    fine = Mesh(mesh.devices.reshape(n_bra, n_ket // (CHIP_X * CORES), CHIP_X, CORES), ("bra",) + KET)
    placed = (
        P(("bra",) + KET, None, None),
        P(("bra",) + KET, None),
        P("bra", KET),
        P(KET, "bra"),
    )
    return jax.shard_map(
        per_device, mesh=fine, in_specs=placed, out_specs=P(KET, "bra"), check_vma=False
    )
```

```python
import jax
import jax.numpy as jnp
from jax import lax
from jax.sharding import Mesh, PartitionSpec as P

RS_MINOR = 256
CHIP_X = 4
CORES = 2
KET = ("y", "x", "core")


def tile_term(amp_block, tile_now):
    return lax.dot_general(
        amp_block,
        tile_now,
        (((1,), (1,)), ((), ())),
        precision=lax.Precision.HIGH,
        preferred_element_type=jnp.float32,
    )


def partial_rows(gathered, integrals, local_rows, row_blocks):
    products = [tile_term(gathered, integrals[s]) for s in range(integrals.shape[0])]
    blocks = []
    for r in range(row_blocks):
        acc = jnp.zeros_like(products[0])
        for s, product in enumerate(products):
            acc = acc + jnp.where(local_rows[s] == r, product, 0.0)
        blocks.append(acc)
    return jnp.concatenate(blocks, axis=1)


def gather_bra(amplitudes):
    n_bra = lax.axis_size("bra")
    copies = jnp.broadcast_to(amplitudes[None], (n_bra,) + amplitudes.shape)
    return lax.all_to_all(copies, "bra", 0, 0, tiled=True).reshape(-1, amplitudes.shape[1])


def reduce_plane(stage):
    got = lax.all_to_all(jnp.transpose(stage, (1, 0, 2)), "x", 0, 0, tiled=True)
    stage = jnp.sum(got, axis=0)
    got = lax.all_to_all(stage, "y", 0, 0, tiled=True)
    return jnp.sum(got, axis=0)


def per_device(integrals, tile_place, amplitudes, denominators):
    tile_width = integrals.shape[1]
    row_blocks = denominators.shape[1] // tile_width
    local_rows = tile_place[:, 0] - lax.axis_index("bra") * row_blocks
    n_y, n_x, n_c = (lax.axis_size(a) for a in KET)
    c = lax.axis_index("core")
    gathered = gather_bra(amplitudes).reshape(n_y, n_x, n_c, -1, tile_width)
    own = lax.dynamic_index_in_dim(gathered, c, axis=2, keepdims=False).reshape(-1, tile_width)
    other = lax.dynamic_index_in_dim(gathered, 1 - c, axis=2, keepdims=False).reshape(-1, tile_width)
    sent = partial_rows(other, integrals, local_rows, row_blocks)
    arrived = lax.ppermute(sent, "core", perm=[(0, 1), (1, 0)])
    stage = partial_rows(own, integrals, local_rows, row_blocks) + arrived
    summed = reduce_plane(stage.reshape(n_y, n_x, -1))
    return summed.reshape(denominators.shape) / denominators


def solution(mesh):
    n_bra, n_ket = mesh.devices.shape
    fine = Mesh(mesh.devices.reshape(n_bra, n_ket // (CHIP_X * CORES), CHIP_X, CORES), ("bra",) + KET)
    placed = (
        P(("bra",) + KET, None, None),
        P(("bra",) + KET, None),
        P("bra", KET),
        P(KET, "bra"),
    )
    return jax.shard_map(
        per_device, mesh=fine, in_specs=placed, out_specs=P(KET, "bra"), check_vma=False
    )
```
